512 devices in a mesh: seq: 32 (over z, y_hi), ep: 16 (over x, y_lo, core).
Axes of the slice: x: 4, y: 4 (y_hi: 2, y_lo: 2; y = y_hi * 2 + y_lo), z: 16, core: 2. Of those that a mesh axis runs over, the one named last changes fastest.
Arguments:
- queries: bfloat16 [12288, 6144], P('seq', 'ep'), may hold values from -5 to 5
- key_heads: bfloat16 [12288, 2048], P('seq', 'ep'), may hold values from -4 to 4, as said below
- value_heads: bfloat16 [12288, 2048], P('seq', 'ep'), may hold values from -6 to 6, as said below
- attn_grad: bfloat16 [12288, 6144], P('seq', 'ep'), may hold values from -6 to 6
- segments: int32 [12288], P('seq'), may hold values from 0 to 63, never falling along the last dimension, each value on 1 to 1153 neighbouring positions
- moe_grad: bfloat16 [12288, 6144], P(('seq', 'ep')), may hold values from -6 to 6
- expert_out: bfloat16 [12288, 2, 6144], P(('seq', 'ep')), may hold values from -6 to 6
- normed: bfloat16 [12288, 6144], P(('seq', 'ep')), may hold values from -6 to 6
- router: bfloat16 [8, 6144], replicated, may hold values from -0.078125 to 0.078125
- routes: int32 [12288, 2], P(('seq', 'ep')), may hold values from 0 to 7, all different within a row; in each aligned block of 24 rows (0 to 23, 24 to 47, ...) at most 6 rows name the same one
Outputs:
- query_grad: bfloat16 [12288, 6144], P('seq', 'ep')
- key_grad: bfloat16 [12288, 2048], P('seq', 'ep')
- value_grad: bfloat16 [12288, 2048], P('seq', 'ep')
- normed_grad: bfloat16 [12288, 6144], P(('seq', 'ep'))
- router_grad: float32 [8, 6144], replicated
- routed_grads: bfloat16 [8192, 6, 6144], P(('seq', 'ep'))
The draws below stay inside these ranges and needn't reach their ends.
Inputs may be any that keep to these rules, and one draw needn't show every extreme that they name: `key_heads`: the 2 indices of ep e with the same e // 2 hold identical copies. `value_heads`: the 2 indices of ep e with the same e // 2 hold identical copies. `segments`: segment numbers never fall along the sequence; every document has 1 to 1153 tokens and one has exactly 1153. A token names two different experts; in each aligned block of 24 tokens (the tokens of one device) every expert is named by exactly 6 routes.
All inputs are finite; a program needn't handle non-finite values.
Results may differ from the reference program's by a relative error of at most 0.0071.
Values may be sent and summed in bfloat16 or wider, within the bound.
No kernel may reach another device: no remote copies, remote signals or barrier semaphores. Data moves between devices by JAX's collectives and lax.ppermute only.
A program may use at most 64 MiB of HBM per device.

```python
import functools
import math
import jax
import jax.numpy as jnp
import numpy as np
from jax import lax

D = 6144
EXPERTS = 8
HD = 128
TOP = 2
REACH = 3
TOK = 384
SEQLEN = 12288
DOC_MOST = 1153
DOCS = 64
QH_DEV = 3
KV_DEV = 1
KV_SHARE = 2
GROUP = 3
MOE_DEV = 24
CAP = 6
EXP_DEV = 1
SPLIT = 2
N_SEQ = 32
N_EP = 16


def copy_heads(base):
    return jnp.repeat(base, KV_SHARE, axis=1)


def draw_key_heads(key, part):
    shape = (SEQLEN, N_EP // KV_SHARE, KV_DEV, HD)
    base = copy_heads(jax.random.truncated_normal(jax.random.fold_in(key, 3), -4.0, 4.0, shape, jnp.float32))
    return base.reshape(SEQLEN, N_EP * KV_DEV * HD).astype(jnp.bfloat16)


def draw_value_heads(key, part):
    shape = (SEQLEN, N_EP // KV_SHARE, KV_DEV, HD)
    base = jax.random.truncated_normal(jax.random.fold_in(key, 7), -6.0, 6.0, shape, jnp.float32)
    return copy_heads(base).reshape(SEQLEN, N_EP * KV_DEV * HD).astype(jnp.bfloat16)


def draw_queries(key, part):
    shape = (SEQLEN, N_EP, KV_DEV, GROUP, HD)
    base = jax.random.truncated_normal(jax.random.fold_in(key, 5), -5.0, 5.0, shape, jnp.float32)
    return base.reshape(SEQLEN, N_EP * KV_DEV * GROUP * HD).astype(jnp.bfloat16)


def steps_of(stream_key, shape, cuts, low, top_value):
    def one(axis_at, parts):
        draws = jax.random.uniform(jax.random.fold_in(jax.random.fold_in(stream_key, 6), axis_at), (parts,), jnp.float32, low / len(cuts), top_value / len(cuts))
        return jnp.repeat(jnp.exp(draws), shape[axis_at] // parts).reshape((-1,) + (1,) * (len(shape) - axis_at - 1))

    gain = one(*cuts[0])
    for cut in cuts[1:]:
        gain = gain * one(*cut)
    return gain


def split_up(amount, total, bound, lean):
    portions = [(1 << 20) // math.isqrt(standing ** lean) + 1 for standing in range(2, amount + 1)]
    surplus, holding = total - bound - (amount - 1), [1] * (amount - 1)
    while surplus > 0:
        movable = [i for i in range(amount - 1) if holding[i] < bound]
        pool, left = sum([portions[i] for i in movable]), surplus
        for i in movable:
            more = min(bound - holding[i], max(1, left * portions[i] // pool), surplus)
            holding[i] = holding[i] + more
            surplus = surplus - more
    return np.array([bound] + holding)


def ragged_sizes(key, amount, total, limit, lean):
    if amount == 2:
        one = jax.random.randint(key, (), max(1, total - limit), min(limit, total - 1) + 1)
        return jnp.stack([one, total - one])
    tallies = jnp.asarray(split_up(amount, total, limit, lean), jnp.int32)
    pairs = (amount - 1) // 2
    giver, taker = tallies[1:1 + 2 * pairs:2], tallies[2:2 + 2 * pairs:2]
    slack = jnp.minimum(giver - 1, limit - taker)
    passed = jax.random.randint(jax.random.fold_in(key, 1), (pairs,), 0, 1 << 20) % (slack + 1)
    tallies = tallies.at[1:1 + 2 * pairs:2].set(giver - passed).at[2:2 + 2 * pairs:2].set(taker + passed)
    return tallies[jax.random.permutation(jax.random.fold_in(key, 2), amount)]


def routed_block(key, own, number, rows, count, top, limit, skew):
    sequence = jax.random.permutation(key, count)
    heavy_load, common = load_shares(count, rows * top, limit, skew, True), load_shares(count, rows * top, limit, skew, False)
    places = jnp.arange(count)

    def named(lengths, offset_by):
        used = int((lengths > 0).sum())
        fixed = max(1, used // 4)
        moved = fixed + (places - fixed + offset_by * (used - fixed)) % max(1, count - fixed)
        return jnp.zeros((count,), jnp.int32).at[sequence[jnp.where(places < fixed, places, moved)]].set(jnp.asarray(lengths, jnp.int32))

    lengths = jnp.where(number % 4 == 0, named(heavy_load, number // 4), named(common, number - number // 4 - 1))
    mixed = jax.random.permutation(jax.random.fold_in(own, 3), count)
    source_of, taker = mixed[0:count // 2 * 2:2], mixed[1:count // 2 * 2:2]
    room = jnp.minimum(lengths[source_of] - 1, limit - lengths[taker]) // 2
    room = jnp.where((source_of == sequence[0]) | (taker == sequence[0]) | (lengths[taker] == 0), 0, jnp.maximum(room, 0))
    moved = jax.random.randint(jax.random.fold_in(own, 4), (count // 2,), 0, 1 << 20) % (room + 1)
    lengths = lengths.at[source_of].add(-moved).at[taker].add(moved)
    items = jnp.searchsorted(jnp.cumsum(lengths), jnp.arange(rows * top), side="right").astype(jnp.int32)
    listing = items.reshape(top, rows).T
    listing = listing[jax.random.permutation(jax.random.fold_in(own, 1), rows)]
    offset_by = jax.random.randint(jax.random.fold_in(own, 2), (rows, 1), 0, top)
    return jnp.take_along_axis(listing, (jnp.arange(top)[None, :] + offset_by) % top, axis=1)


def load_shares(count, total, bound, skew, full):
    weights = [(1 << 20) // math.isqrt(standing ** skew) + 1 for standing in range(1, count + 1)]
    largest = bound if full else min(bound, max(-(-total // count), total * weights[0] // sum(weights)))
    least = 1 if total - largest >= count - 1 else 0
    given, surplus = [largest] + [least] * (count - 1), total - largest - least * (count - 1)
    while surplus > 0:
        movable = [i for i in range(1, count) if given[i] < largest] or [i for i in range(1, count) if given[i] < bound]
        mass, budget = sum([weights[i] for i in movable]), surplus
        for i in movable:
            addition = min(bound - given[i], max(1, budget * weights[i] // mass), surplus)
            given[i] = given[i] + addition
            surplus = surplus - addition
    return np.array(given)


def centred(stream_key, shape, scale, most, pieces=(), kind=jnp.bfloat16):
    values = jax.random.normal(stream_key, shape, jnp.float32) * scale
    if len(pieces) > 0:
        values = steps_of(stream_key, shape, pieces, -0.22, 0.18) * values
    return jnp.clip(values, min=-most, max=most).astype(kind)


def setup_inputs(seed: int = 0) -> dict:
    key_list = jax.random.split(jax.random.key(seed), 11)
    queries = draw_queries(jax.random.fold_in(key_list[10], 71), 0)
    key_heads = draw_key_heads(jax.random.fold_in(key_list[10], 71), 0)
    value_heads = draw_value_heads(jax.random.fold_in(key_list[10], 71), 0)
    attn_grad = centred(key_list[3], (SEQLEN, N_EP * QH_DEV * HD), 1.0, 6.0, ((0, 32), (1, 16)))
    segments = jnp.searchsorted(jnp.cumsum(ragged_sizes(key_list[4], DOCS, SEQLEN, DOC_MOST, 1)), jnp.arange(SEQLEN), side="right").astype(jnp.int32)
    moe_grad = centred(key_list[5], (SEQLEN, D), 1.0, 6.0, ((0, 512),))
    expert_out = centred(key_list[6], (SEQLEN, TOP, D), 1.0, 6.0, ((0, 512),))
    normed = centred(key_list[7], (SEQLEN, D), 1.0, 6.0, ((0, 512),))
    router = centred(key_list[8], (EXPERTS, D), D ** -0.5, 0.078125)
    routes_keys = jax.random.split(jax.random.fold_in(key_list[9], 1), SEQLEN // MOE_DEV)
    routes_turns = jax.random.permutation(jax.random.fold_in(key_list[9], 3), SEQLEN // MOE_DEV)
    routes = jax.vmap(lambda own, number: routed_block(jax.random.fold_in(key_list[9], 2), own, number, MOE_DEV, EXPERTS, TOP, CAP, 0))(routes_keys, routes_turns).reshape((SEQLEN, TOP))
    return {"queries": queries, "key_heads": key_heads, "value_heads": value_heads, "attn_grad": attn_grad, "segments": segments, "moe_grad": moe_grad, "expert_out": expert_out, "normed": normed, "router": router, "routes": routes}


MASKED = -1e+30

def attention_grads(queries, key_heads, value_heads, attn_grad, segments):
    score_scale = 1.0 / math.sqrt(HD)
    num_blocks = SEQLEN // TOK
    query_all = queries.astype(jnp.float32).reshape(num_blocks, TOK, N_EP, KV_DEV, GROUP, HD)
    grad_all = attn_grad.astype(jnp.float32).reshape(num_blocks, TOK, N_EP, KV_DEV, GROUP, HD)
    key_all = key_heads.astype(jnp.float32).reshape(num_blocks, TOK, N_EP, KV_DEV, HD)
    value_all = value_heads.astype(jnp.float32).reshape(num_blocks, TOK, N_EP, KV_DEV, HD)
    seg_all = segments.reshape(num_blocks, TOK)
    positions = jnp.arange(TOK, dtype=jnp.int32)

    def allowed(row_block, col_block):
        clipped = jnp.maximum(col_block, 0)
        row_pos = row_block * TOK + positions
        col_pos = col_block * TOK + positions
        same_doc = seg_all[row_block][:, None] == seg_all[clipped][None, :]
        return same_doc & (col_pos[None, :] <= row_pos[:, None]) & (col_block >= 0)

    def is_live(row_block, col_block):
        clipped = jnp.maximum(col_block, 0)
        return (col_block >= 0) & (seg_all[clipped][TOK - 1] >= seg_all[row_block][0])

    def scores_and_grad(row_block, col_block):
        clipped = jnp.maximum(col_block, 0)
        mask = allowed(row_block, col_block)
        raw_scores = jnp.einsum('qehgd,tehd->ehgqt', query_all[row_block], key_all[clipped]) * score_scale
        scores = jnp.where(mask, raw_scores, MASKED)
        prob_grad = jnp.einsum('qehgd,tehd->ehgqt', grad_all[row_block], value_all[clipped])
        return (mask, scores, prob_grad)

    def stats_block(row_block, col_block, running):
        row_peak, row_total, weighted = running
        mask, scores, prob_grad = scores_and_grad(row_block, col_block)
        new_peak = jnp.maximum(row_peak, lax.optimization_barrier(jnp.max(scores, axis=-1)))
        factor = jnp.exp(row_peak - new_peak)
        weights = jnp.where(mask, jnp.exp(scores - new_peak[..., None]), 0.0)
        return (new_peak, row_total * factor + lax.optimization_barrier(jnp.sum(weights, axis=-1)), weighted * factor + lax.optimization_barrier(jnp.sum(weights * prob_grad, axis=-1)))

    def grad_block(row_block, col_block, log_total, delta, carried):
        query_acc, key_acc, value_acc = carried
        clipped = jnp.maximum(col_block, 0)
        mask, scores, prob_grad = scores_and_grad(row_block, col_block)
        soft_probs = jnp.where(mask, jnp.exp(scores - log_total[..., None]), 0.0)
        probs_low = lax.optimization_barrier(soft_probs.astype(jnp.bfloat16)).astype(jnp.float32)
        value_part = jnp.einsum('ehgqt,qehgd->tehd', probs_low, grad_all[row_block])
        score_low = lax.optimization_barrier((soft_probs * (prob_grad - delta[..., None])).astype(jnp.bfloat16)).astype(jnp.float32)
        query_part = jnp.einsum('ehgqt,tehd->qehgd', score_low, key_all[clipped]) * score_scale
        key_part = jnp.einsum('ehgqt,qehgd->tehd', score_low, query_all[row_block]) * score_scale
        return (query_acc + query_part, key_acc.at[clipped].add(key_part), value_acc.at[clipped].add(value_part))

    def scan_step(carried, row_block):
        key_acc, value_acc = carried
        stat_shape = (N_EP, KV_DEV, GROUP, TOK)
        running = (jnp.full(stat_shape, MASKED, jnp.float32), jnp.zeros(stat_shape, jnp.float32), jnp.zeros(stat_shape, jnp.float32))
        for offset in range(REACH + 1):
            col_block = row_block - offset
            running = lax.cond(is_live(row_block, col_block), functools.partial(stats_block, row_block, col_block), lambda unchanged: unchanged, running)
        row_peak, row_total, weighted = running
        log_total = row_peak + jnp.log(row_total)
        delta = weighted / row_total
        accs = (jnp.zeros((TOK, N_EP, KV_DEV, GROUP, HD), jnp.float32), key_acc, value_acc)
        for offset in range(REACH + 1):
            col_block = row_block - offset
            accs = lax.cond(is_live(row_block, col_block), functools.partial(grad_block, row_block, col_block, log_total, delta), lambda unchanged: unchanged, accs)
        return ((accs[1], accs[2]), accs[0])
    zero_keys = jnp.zeros((num_blocks, TOK, N_EP, KV_DEV, HD), jnp.float32)
    (key_acc, value_acc), query_blocks = lax.scan(scan_step, (zero_keys, zero_keys), jnp.arange(num_blocks, dtype=jnp.int32))
    query_grad = query_blocks.reshape(SEQLEN, N_EP * QH_DEV * HD).astype(jnp.bfloat16)
    key_grad = key_acc.reshape(SEQLEN, N_EP * KV_DEV * HD).astype(jnp.bfloat16)
    value_grad = value_acc.reshape(SEQLEN, N_EP * KV_DEV * HD).astype(jnp.bfloat16)
    return (query_grad, key_grad, value_grad)

def router_grads(moe_grad, expert_out, normed, router, routes):
    logits = jnp.einsum('td,ed->te', normed.astype(jnp.float32), router.astype(jnp.float32))
    expert_ids = jnp.arange(EXPERTS, dtype=jnp.int32)
    onehot = (routes[:, :, None] == expert_ids[None, None, :]).astype(jnp.float32)
    chosen = lax.optimization_barrier(jnp.sum(onehot * logits[:, None, :], axis=2))
    first_gate = 1.0 / (1.0 + jnp.exp(chosen[:, 1] - chosen[:, 0]))
    second_gate = 1.0 - first_gate
    gate_grad = jnp.einsum('td,tkd->tk', moe_grad.astype(jnp.float32), expert_out.astype(jnp.float32))
    logit_step = first_gate * second_gate * (gate_grad[:, 0] - gate_grad[:, 1])
    logit_grad = (onehot[:, 0, :] - onehot[:, 1, :]) * logit_step[:, None]
    normed_grad = jnp.dot(logit_grad, router.astype(jnp.float32), precision=lax.Precision.HIGHEST).astype(jnp.bfloat16)
    router_grad = jnp.dot(logit_grad.T, normed.astype(jnp.float32), precision=lax.Precision.HIGHEST) / SEQLEN
    gates = jnp.stack([first_gate, second_gate], axis=1)
    expert_rows = (gates[:, :, None] * moe_grad.astype(jnp.float32)[:, None, :]).astype(jnp.bfloat16)
    num_blocks = SEQLEN // MOE_DEV
    route_count = MOE_DEV * TOP
    flat_routes = routes.reshape(num_blocks, route_count)
    hot = (flat_routes[:, :, None] == expert_ids[None, None, :]).astype(jnp.int32)
    ranks = lax.optimization_barrier(jnp.sum((jnp.cumsum(hot, axis=1) - 1) * hot, axis=2))
    order = jnp.argsort(flat_routes * CAP + ranks, axis=1).astype(jnp.int32)
    global_index = order + (jnp.arange(num_blocks, dtype=jnp.int32) * route_count)[:, None]
    slot_index = global_index.reshape(N_SEQ, N_EP, EXPERTS, CAP)
    slot_index = jnp.repeat(slot_index, SPLIT, axis=2).reshape(N_SEQ, N_EP, N_EP, EXP_DEV * CAP)
    slot_index = jnp.transpose(slot_index, (0, 2, 1, 3)).reshape(N_SEQ * N_EP * N_EP, EXP_DEV * CAP)
    routed_grads = expert_rows.reshape(SEQLEN * TOP, D)[slot_index]
    return (normed_grad, router_grad, routed_grads)

def reference(queries, key_heads, value_heads, attn_grad, segments, moe_grad, expert_out, normed, router, routes):
    query_grad, key_grad, value_grad = attention_grads(queries, key_heads, value_heads, attn_grad, segments)
    normed_grad, router_grad, routed_grads = router_grads(moe_grad, expert_out, normed, router, routes)
    return (query_grad, key_grad, value_grad, normed_grad, router_grad, routed_grads)
```

```python
import functools
import math

import jax
import jax.numpy as jnp
from jax import lax
from jax.sharding import PartitionSpec as P

EXPERTS = 8
HD = 128
TOP = 2
REACH = 3


MASKED = -1e30


def from_behind(value, axis, by):
    devices = lax.axis_size(axis)
    pairs = [(i, i + by) for i in range(devices) if 0 <= i + by < devices]
    return lax.ppermute(value, axis, pairs)


def scatter_sum(flat, axis):
    parts = flat.reshape(lax.axis_size(axis), -1)
    return lax.all_to_all(parts, axis, 0, 0, tiled=True).sum(axis=0)


def gather_back(flat, axis):
    copies = jnp.broadcast_to(flat[None], (lax.axis_size(axis),) + flat.shape)
    return lax.all_to_all(copies, axis, 0, 0, tiled=True).reshape(-1)


def sum_everywhere(value):
    flat = scatter_sum(scatter_sum(value.reshape(-1), "ep"), "seq")
    return gather_back(gather_back(flat, "seq"), "ep").reshape(value.shape)


def allowed_pairs(seg_rows, seg_keys, seq_index, offset, tok_rows):
    positions = jnp.arange(tok_rows, dtype=jnp.int32)
    row_pos = seq_index * tok_rows + positions
    key_pos = (seq_index - offset) * tok_rows + positions
    same_doc = seg_rows[:, None] == seg_keys[None, :]
    causal = key_pos[None, :] <= row_pos[:, None]
    return same_doc & causal & (seq_index - offset >= 0)


def masked_scores(query_rows, key_block, allowed, score_scale):
    raw_scores = (
        jnp.einsum("qhgd,thd->hgqt", query_rows, key_block, preferred_element_type=jnp.float32)
        * score_scale
    )
    return jnp.where(allowed, raw_scores, MASKED)


def stats_update(running, query_rows, grad_rows, key_block, value_block, allowed, score_scale):
    row_peak, row_total, weighted = running
    scores = masked_scores(query_rows, key_block, allowed, score_scale)
    prob_grad = jnp.einsum(
        "qhgd,thd->hgqt", grad_rows, value_block, preferred_element_type=jnp.float32
    )
    new_peak = jnp.maximum(row_peak, jnp.max(scores, axis=-1))
    factor = jnp.exp(row_peak - new_peak)
    weights = jnp.where(allowed, jnp.exp(scores - new_peak[..., None]), 0.0)
    return (
        new_peak,
        row_total * factor + jnp.sum(weights, axis=-1),
        weighted * factor + jnp.sum(weights * prob_grad, axis=-1),
    )


def block_grads(
    query_rows, grad_rows, key_block, value_block, allowed, log_total, delta, score_scale
):
    scores = masked_scores(query_rows, key_block, allowed, score_scale)
    soft_probs = jnp.where(allowed, jnp.exp(scores - log_total[..., None]), 0.0)
    probs_low = soft_probs.astype(jnp.bfloat16)
    value_part = jnp.einsum(
        "hgqt,qhgd->thd", probs_low, grad_rows, preferred_element_type=jnp.float32
    )
    prob_grad = jnp.einsum(
        "qhgd,thd->hgqt", grad_rows, value_block, preferred_element_type=jnp.float32
    )
    score_low = (soft_probs * (prob_grad - delta[..., None])).astype(jnp.bfloat16)
    query_part = (
        jnp.einsum("hgqt,thd->qhgd", score_low, key_block, preferred_element_type=jnp.float32)
        * score_scale
    )
    key_part = (
        jnp.einsum("hgqt,qhgd->thd", score_low, query_rows, preferred_element_type=jnp.float32)
        * score_scale
    )
    return (query_part, key_part, value_part)


def on_device(
    queries,
    key_heads,
    value_heads,
    attn_grad,
    segments,
    moe_grad,
    expert_out,
    normed,
    router,
    routes,
):
    tok_rows = queries.shape[0]
    kv_heads = key_heads.shape[1] // HD
    group_size = queries.shape[1] // (kv_heads * HD)
    score_scale = 1.0 / math.sqrt(HD)
    query_rows = queries.reshape(tok_rows, kv_heads, group_size, HD)
    grad_rows = attn_grad.reshape(tok_rows, kv_heads, group_size, HD)
    key_block = key_heads.reshape(tok_rows, kv_heads, HD)
    value_block = value_heads.reshape(tok_rows, kv_heads, HD)
    seq_index = lax.axis_index("seq")
    ep_size = lax.axis_size("ep")
    gathered = [(key_block, value_block, segments)]
    for offset in range(1, REACH + 1):
        gathered.append(from_behind((key_block, value_block, segments), "seq", offset))
    stat_shape = (kv_heads, group_size, tok_rows)
    running = (
        jnp.full(stat_shape, MASKED, jnp.float32),
        jnp.zeros(stat_shape, jnp.float32),
        jnp.zeros(stat_shape, jnp.float32),
    )
    masks = []
    for offset, (keys_now, values_now, segs_now) in enumerate(gathered):
        allowed = allowed_pairs(segments, segs_now, seq_index, offset, tok_rows)
        masks.append(allowed)
        compute = functools.partial(
            stats_update, running, query_rows, grad_rows, keys_now, values_now, allowed, score_scale
        )
        if offset == 0:
            running = compute()
        else:
            running = compute()
    row_peak, row_total, weighted = running
    log_total = row_peak + jnp.log(row_total)
    delta = weighted / row_total
    parts = []
    for offset, (keys_now, values_now, segs_now) in enumerate(gathered):
        compute = functools.partial(
            block_grads,
            query_rows,
            grad_rows,
            keys_now,
            values_now,
            masks[offset],
            log_total,
            delta,
            score_scale,
        )
        if offset == 0:
            parts.append(compute())
        else:
            parts.append(compute())
    query_total = parts[0][0]
    for offset in range(1, REACH + 1):
        query_total = query_total + parts[offset][0]
    key_total = parts[0][1]
    value_total = parts[0][2]
    for offset in range(1, REACH + 1):
        key_back, value_back = from_behind((parts[offset][1], parts[offset][2]), "seq", -offset)
        key_total = key_total + key_back
        value_total = value_total + value_back
    query_grad = query_total.reshape(tok_rows, -1).astype(jnp.bfloat16)
    key_grad = key_total.reshape(tok_rows, -1).astype(jnp.bfloat16)
    value_grad = value_total.reshape(tok_rows, -1).astype(jnp.bfloat16)
    moe_rows = moe_grad.shape[0]
    capacity = moe_rows * TOP // EXPERTS
    copies = max(1, ep_size // EXPERTS)
    logits = jnp.einsum("td,ed->te", normed, router, preferred_element_type=jnp.float32)
    expert_ids = jnp.arange(EXPERTS, dtype=jnp.int32)
    onehot = (routes[:, :, None] == expert_ids[None, None, :]).astype(jnp.float32)
    chosen = jnp.sum(onehot * logits[:, None, :], axis=2)
    first_gate = 1.0 / (1.0 + jnp.exp(chosen[:, 1] - chosen[:, 0]))
    second_gate = 1.0 - first_gate
    gate_grad = jnp.einsum("td,tkd->tk", moe_grad, expert_out, preferred_element_type=jnp.float32)
    logit_step = first_gate * second_gate * (gate_grad[:, 0] - gate_grad[:, 1])
    logit_grad = (onehot[:, 0, :] - onehot[:, 1, :]) * logit_step[:, None]
    normed_grad = jnp.dot(
        logit_grad, router.astype(jnp.float32), precision=lax.Precision.HIGHEST
    ).astype(jnp.bfloat16)
    local_router = jnp.dot(
        logit_grad.T, normed.astype(jnp.float32), precision=lax.Precision.HIGHEST
    )
    all_tokens = moe_rows * lax.axis_size("seq") * ep_size
    router_grad = sum_everywhere(local_router) / all_tokens
    gates = jnp.stack([first_gate, second_gate], axis=1)
    expert_rows = (gates[:, :, None] * moe_grad.astype(jnp.float32)[:, None, :]).astype(
        jnp.bfloat16
    )
    flat_routes = routes.reshape(-1)
    hot = (flat_routes[:, None] == expert_ids[None, :]).astype(jnp.int32)
    ranks = jnp.sum((jnp.cumsum(hot, axis=0) - 1) * hot, axis=1)
    order = jnp.argsort(flat_routes * capacity + ranks)
    outgoing = expert_rows.reshape(-1, expert_rows.shape[2])[order]
    outgoing = jnp.repeat(outgoing.reshape(EXPERTS, capacity, -1), copies, axis=0)
    routed_grads = lax.all_to_all(outgoing, "ep", split_axis=0, concat_axis=0, tiled=True)
    return (query_grad, key_grad, value_grad, normed_grad, router_grad, routed_grads)


def solution(mesh):
    return jax.shard_map(
        on_device,
        mesh=mesh,
        in_specs=(
            P("seq", "ep"),
            P("seq", "ep"),
            P("seq", "ep"),
            P("seq", "ep"),
            P("seq"),
            P(("seq", "ep"), None),
            P(("seq", "ep"), None, None),
            P(("seq", "ep"), None),
            P(),
            P(("seq", "ep"), None),
        ),
        out_specs=(
            P("seq", "ep"),
            P("seq", "ep"),
            P("seq", "ep"),
            P(("seq", "ep"), None),
            P(),
            P(("seq", "ep"), None, None),
        ),
        check_vma=False,
    )
```

```python
import functools
import math

import jax
import jax.numpy as jnp
from jax import lax
from jax.sharding import PartitionSpec as P

EXPERTS = 8
HD = 128
TOP = 2
REACH = 3


MASKED = -1e30


def from_behind(value, axis, by):
    devices = lax.axis_size(axis)
    pairs = [(i, i + by) for i in range(devices) if 0 <= i + by < devices]
    return lax.ppermute(value, axis, pairs)


def pack_block(key_block, value_block, segments):
    tok_rows = key_block.shape[0]
    width = 2 * key_block.shape[1] * HD
    rows = jnp.concatenate([key_block, value_block], axis=-1).reshape(tok_rows, width)
    segs = segments.astype(jnp.bfloat16).reshape(-1, HD)
    segs = jnp.pad(segs, ((0, 8 - segs.shape[0] % 8), (0, width - HD)))
    return jnp.concatenate([rows, segs], axis=0)


def unpack_block(packed, tok_rows, kv_heads):
    rows = packed[:tok_rows].reshape(tok_rows, kv_heads, 2 * HD)
    segs = packed[tok_rows : tok_rows + tok_rows // HD, :HD].reshape(tok_rows)
    return rows[..., :HD], rows[..., HD:], segs.astype(jnp.int32)


def scatter_sum(flat, axis):
    parts = flat.reshape(lax.axis_size(axis), -1)
    return lax.all_to_all(parts, axis, 0, 0, tiled=True).sum(axis=0)


def gather_back(flat, axis):
    copies = jnp.broadcast_to(flat[None], (lax.axis_size(axis),) + flat.shape)
    return lax.all_to_all(copies, axis, 0, 0, tiled=True).reshape(-1)


def sum_everywhere(value):
    flat = scatter_sum(scatter_sum(value.reshape(-1), "ep"), "seq")
    return gather_back(gather_back(flat, "seq"), "ep").reshape(value.shape)


def allowed_pairs(seg_rows, seg_keys, seq_index, offset, tok_rows):
    positions = jnp.arange(tok_rows, dtype=jnp.int32)
    row_pos = seq_index * tok_rows + positions
    key_pos = (seq_index - offset) * tok_rows + positions
    same_doc = seg_rows[:, None] == seg_keys[None, :]
    causal = key_pos[None, :] <= row_pos[:, None]
    return same_doc & causal & (seq_index - offset >= 0)


def masked_scores(query_rows, key_block, allowed, score_scale):
    raw_scores = (
        jnp.einsum("qhgd,thd->hgqt", query_rows, key_block, preferred_element_type=jnp.float32)
        * score_scale
    )
    return jnp.where(allowed, raw_scores, MASKED)


def stats_update(running, query_rows, grad_rows, key_block, value_block, allowed, score_scale):
    row_peak, row_total, weighted = running
    scores = masked_scores(query_rows, key_block, allowed, score_scale)
    prob_grad = jnp.einsum(
        "qhgd,thd->hgqt", grad_rows, value_block, preferred_element_type=jnp.float32
    )
    new_peak = jnp.maximum(row_peak, jnp.max(scores, axis=-1))
    factor = jnp.exp(row_peak - new_peak)
    weights = jnp.where(allowed, jnp.exp(scores - new_peak[..., None]), 0.0)
    return (
        new_peak,
        row_total * factor + jnp.sum(weights, axis=-1),
        weighted * factor + jnp.sum(weights * prob_grad, axis=-1),
    )


def block_grads(
    query_rows, grad_rows, key_block, value_block, allowed, log_total, delta, score_scale
):
    scores = masked_scores(query_rows, key_block, allowed, score_scale)
    soft_probs = jnp.where(allowed, jnp.exp(scores - log_total[..., None]), 0.0)
    probs_low = soft_probs.astype(jnp.bfloat16)
    value_part = jnp.einsum(
        "hgqt,qhgd->thd", probs_low, grad_rows, preferred_element_type=jnp.float32
    )
    prob_grad = jnp.einsum(
        "qhgd,thd->hgqt", grad_rows, value_block, preferred_element_type=jnp.float32
    )
    score_low = (soft_probs * (prob_grad - delta[..., None])).astype(jnp.bfloat16)
    query_part = (
        jnp.einsum("hgqt,thd->qhgd", score_low, key_block, preferred_element_type=jnp.float32)
        * score_scale
    )
    key_part = (
        jnp.einsum("hgqt,qhgd->thd", score_low, query_rows, preferred_element_type=jnp.float32)
        * score_scale
    )
    return (query_part, key_part, value_part)


def on_device(
    queries,
    key_heads,
    value_heads,
    attn_grad,
    segments,
    moe_grad,
    expert_out,
    normed,
    router,
    routes,
):
    tok_rows = queries.shape[0]
    kv_heads = key_heads.shape[1] // HD
    group_size = queries.shape[1] // (kv_heads * HD)
    score_scale = 1.0 / math.sqrt(HD)
    query_rows = queries.reshape(tok_rows, kv_heads, group_size, HD)
    grad_rows = attn_grad.reshape(tok_rows, kv_heads, group_size, HD)
    key_block = key_heads.reshape(tok_rows, kv_heads, HD)
    value_block = value_heads.reshape(tok_rows, kv_heads, HD)
    seq_index = lax.axis_index("seq")
    ep_size = lax.axis_size("ep")
    gathered = [(key_block, value_block, segments)]
    packed = pack_block(key_block, value_block, segments)
    for offset in range(1, REACH + 1):
        gathered.append(unpack_block(from_behind(packed, "seq", offset), tok_rows, kv_heads))
    stat_shape = (kv_heads, group_size, tok_rows)
    running = (
        jnp.full(stat_shape, MASKED, jnp.float32),
        jnp.zeros(stat_shape, jnp.float32),
        jnp.zeros(stat_shape, jnp.float32),
    )
    masks = []
    for offset, (keys_now, values_now, segs_now) in enumerate(gathered):
        allowed = allowed_pairs(segments, segs_now, seq_index, offset, tok_rows)
        masks.append(allowed)
        compute = functools.partial(
            stats_update, running, query_rows, grad_rows, keys_now, values_now, allowed, score_scale
        )
        if offset == 0:
            running = compute()
        else:
            running = compute()
    row_peak, row_total, weighted = running
    log_total = row_peak + jnp.log(row_total)
    delta = weighted / row_total
    parts = []
    for offset, (keys_now, values_now, segs_now) in enumerate(gathered):
        compute = functools.partial(
            block_grads,
            query_rows,
            grad_rows,
            keys_now,
            values_now,
            masks[offset],
            log_total,
            delta,
            score_scale,
        )
        if offset == 0:
            parts.append(compute())
        else:
            parts.append(compute())
    query_total = parts[0][0]
    for offset in range(1, REACH + 1):
        query_total = query_total + parts[offset][0]
    key_total = parts[0][1]
    value_total = parts[0][2]
    for offset in range(1, REACH + 1):
        both = jnp.concatenate([parts[offset][1], parts[offset][2]], axis=-1)
        both = from_behind(both, "seq", -offset)
        key_back, value_back = both[..., :HD], both[..., HD:]
        key_total = key_total + key_back
        value_total = value_total + value_back
    query_grad = query_total.reshape(tok_rows, -1).astype(jnp.bfloat16)
    key_grad = key_total.reshape(tok_rows, -1).astype(jnp.bfloat16)
    value_grad = value_total.reshape(tok_rows, -1).astype(jnp.bfloat16)
    moe_rows = moe_grad.shape[0]
    capacity = moe_rows * TOP // EXPERTS
    copies = max(1, ep_size // EXPERTS)
    logits = jnp.einsum("td,ed->te", normed, router, preferred_element_type=jnp.float32)
    expert_ids = jnp.arange(EXPERTS, dtype=jnp.int32)
    onehot = (routes[:, :, None] == expert_ids[None, None, :]).astype(jnp.float32)
    chosen = jnp.sum(onehot * logits[:, None, :], axis=2)
    first_gate = 1.0 / (1.0 + jnp.exp(chosen[:, 1] - chosen[:, 0]))
    second_gate = 1.0 - first_gate
    gate_grad = jnp.einsum("td,tkd->tk", moe_grad, expert_out, preferred_element_type=jnp.float32)
    logit_step = first_gate * second_gate * (gate_grad[:, 0] - gate_grad[:, 1])
    logit_grad = (onehot[:, 0, :] - onehot[:, 1, :]) * logit_step[:, None]
    normed_grad = jnp.dot(
        logit_grad, router.astype(jnp.float32), precision=lax.Precision.HIGHEST
    ).astype(jnp.bfloat16)
    local_router = jnp.dot(
        logit_grad.T, normed.astype(jnp.float32), precision=lax.Precision.HIGHEST
    )
    all_tokens = moe_rows * lax.axis_size("seq") * ep_size
    router_grad = sum_everywhere(local_router) / all_tokens
    gates = jnp.stack([first_gate, second_gate], axis=1)
    expert_rows = (gates[:, :, None] * moe_grad.astype(jnp.float32)[:, None, :]).astype(
        jnp.bfloat16
    )
    flat_routes = routes.reshape(-1)
    hot = (flat_routes[:, None] == expert_ids[None, :]).astype(jnp.int32)
    ranks = jnp.sum((jnp.cumsum(hot, axis=0) - 1) * hot, axis=1)
    order = jnp.argsort(flat_routes * capacity + ranks)
    outgoing = expert_rows.reshape(-1, expert_rows.shape[2])[order]
    outgoing = jnp.repeat(outgoing.reshape(EXPERTS, capacity, -1), copies, axis=0)
    routed_grads = lax.all_to_all(outgoing, "ep", split_axis=0, concat_axis=0, tiled=True)
    return (query_grad, key_grad, value_grad, normed_grad, router_grad, routed_grads)


def solution(mesh):
    return jax.shard_map(
        on_device,
        mesh=mesh,
        in_specs=(
            P("seq", "ep"),
            P("seq", "ep"),
            P("seq", "ep"),
            P("seq", "ep"),
            P("seq"),
            P(("seq", "ep"), None),
            P(("seq", "ep"), None, None),
            P(("seq", "ep"), None),
            P(),
            P(("seq", "ep"), None),
        ),
        out_specs=(
            P("seq", "ep"),
            P("seq", "ep"),
            P("seq", "ep"),
            P(("seq", "ep"), None),
            P(),
            P(("seq", "ep"), None, None),
        ),
        check_vma=False,
    )
```

```python
import functools
import math

import jax
import jax.numpy as jnp
from jax import lax
from jax.sharding import PartitionSpec as P

EXPERTS = 8
HD = 128
TOP = 2
REACH = 3


MASKED = -1e30


def from_behind(value, axis, by):
    devices = lax.axis_size(axis)
    pairs = [(i, i + by) for i in range(devices) if 0 <= i + by < devices]
    return lax.ppermute(value, axis, pairs)


def pack_block(key_block, value_block, segments):
    tok_rows = key_block.shape[0]
    width = 2 * key_block.shape[1] * HD
    rows = jnp.concatenate([key_block, value_block], axis=-1).reshape(tok_rows, width)
    segs = segments.astype(jnp.bfloat16).reshape(-1, HD)
    segs = jnp.pad(segs, ((0, 8 - segs.shape[0] % 8), (0, width - HD)))
    return jnp.concatenate([rows, segs], axis=0)


def unpack_block(packed, tok_rows, kv_heads):
    rows = packed[:tok_rows].reshape(tok_rows, kv_heads, 2 * HD)
    segs = packed[tok_rows : tok_rows + tok_rows // HD, :HD].reshape(tok_rows)
    return rows[..., :HD], rows[..., HD:], segs.astype(jnp.int32)


def scatter_sum(flat, axis):
    parts = flat.reshape(lax.axis_size(axis), -1)
    return lax.all_to_all(parts, axis, 0, 0, tiled=True).sum(axis=0)


def gather_back(flat, axis):
    copies = jnp.broadcast_to(flat[None], (lax.axis_size(axis),) + flat.shape)
    return lax.all_to_all(copies, axis, 0, 0, tiled=True).reshape(-1)


def broadcast_sum(flat, axis):
    copies = jnp.broadcast_to(flat[None], (lax.axis_size(axis),) + flat.shape)
    return lax.all_to_all(copies, axis, 0, 0, tiled=True).sum(axis=0)


def sum_everywhere(value):
    flat = broadcast_sum(scatter_sum(value.reshape(-1), "ep"), "seq")
    return gather_back(flat, "ep").reshape(value.shape)


def allowed_pairs(seg_rows, seg_keys, seq_index, offset, tok_rows):
    positions = jnp.arange(tok_rows, dtype=jnp.int32)
    row_pos = seq_index * tok_rows + positions
    key_pos = (seq_index - offset) * tok_rows + positions
    same_doc = seg_rows[:, None] == seg_keys[None, :]
    causal = key_pos[None, :] <= row_pos[:, None]
    return same_doc & causal & (seq_index - offset >= 0)


def masked_scores(query_rows, key_block, allowed, score_scale):
    raw_scores = (
        jnp.einsum("qhgd,thd->hgqt", query_rows, key_block, preferred_element_type=jnp.float32)
        * score_scale
    )
    return jnp.where(allowed, raw_scores, MASKED)


def stats_update(running, query_rows, grad_rows, key_block, value_block, allowed, score_scale):
    row_peak, row_total, weighted = running
    scores = masked_scores(query_rows, key_block, allowed, score_scale)
    prob_grad = jnp.einsum(
        "qhgd,thd->hgqt", grad_rows, value_block, preferred_element_type=jnp.float32
    )
    new_peak = jnp.maximum(row_peak, jnp.max(scores, axis=-1))
    factor = jnp.exp(row_peak - new_peak)
    weights = jnp.where(allowed, jnp.exp(scores - new_peak[..., None]), 0.0)
    return (
        new_peak,
        row_total * factor + jnp.sum(weights, axis=-1),
        weighted * factor + jnp.sum(weights * prob_grad, axis=-1),
    )


def block_grads(
    query_rows, grad_rows, key_block, value_block, allowed, log_total, delta, score_scale
):
    scores = masked_scores(query_rows, key_block, allowed, score_scale)
    soft_probs = jnp.where(allowed, jnp.exp(scores - log_total[..., None]), 0.0)
    probs_low = soft_probs.astype(jnp.bfloat16)
    value_part = jnp.einsum(
        "hgqt,qhgd->thd", probs_low, grad_rows, preferred_element_type=jnp.float32
    )
    prob_grad = jnp.einsum(
        "qhgd,thd->hgqt", grad_rows, value_block, preferred_element_type=jnp.float32
    )
    score_low = (soft_probs * (prob_grad - delta[..., None])).astype(jnp.bfloat16)
    query_part = (
        jnp.einsum("hgqt,thd->qhgd", score_low, key_block, preferred_element_type=jnp.float32)
        * score_scale
    )
    key_part = (
        jnp.einsum("hgqt,qhgd->thd", score_low, query_rows, preferred_element_type=jnp.float32)
        * score_scale
    )
    return (query_part, key_part, value_part)


def on_device(
    queries,
    key_heads,
    value_heads,
    attn_grad,
    segments,
    moe_grad,
    expert_out,
    normed,
    router,
    routes,
):
    tok_rows = queries.shape[0]
    kv_heads = key_heads.shape[1] // HD
    group_size = queries.shape[1] // (kv_heads * HD)
    score_scale = 1.0 / math.sqrt(HD)
    query_rows = queries.reshape(tok_rows, kv_heads, group_size, HD)
    grad_rows = attn_grad.reshape(tok_rows, kv_heads, group_size, HD)
    key_block = key_heads.reshape(tok_rows, kv_heads, HD)
    value_block = value_heads.reshape(tok_rows, kv_heads, HD)
    seq_index = lax.axis_index("seq")
    ep_size = lax.axis_size("ep")
    gathered = [(key_block, value_block, segments)]
    packed = pack_block(key_block, value_block, segments)
    for offset in range(1, REACH + 1):
        gathered.append(unpack_block(from_behind(packed, "seq", offset), tok_rows, kv_heads))
    stat_shape = (kv_heads, group_size, tok_rows)
    running = (
        jnp.full(stat_shape, MASKED, jnp.float32),
        jnp.zeros(stat_shape, jnp.float32),
        jnp.zeros(stat_shape, jnp.float32),
    )
    masks = []
    for offset, (keys_now, values_now, segs_now) in enumerate(gathered):
        allowed = allowed_pairs(segments, segs_now, seq_index, offset, tok_rows)
        masks.append(allowed)
        compute = functools.partial(
            stats_update, running, query_rows, grad_rows, keys_now, values_now, allowed, score_scale
        )
        if offset == 0:
            running = compute()
        else:
            running = compute()
    row_peak, row_total, weighted = running
    log_total = row_peak + jnp.log(row_total)
    delta = weighted / row_total
    parts = []
    for offset, (keys_now, values_now, segs_now) in enumerate(gathered):
        compute = functools.partial(
            block_grads,
            query_rows,
            grad_rows,
            keys_now,
            values_now,
            masks[offset],
            log_total,
            delta,
            score_scale,
        )
        if offset == 0:
            parts.append(compute())
        else:
            parts.append(compute())
    query_total = parts[0][0]
    for offset in range(1, REACH + 1):
        query_total = query_total + parts[offset][0]
    key_total = parts[0][1]
    value_total = parts[0][2]
    for offset in range(1, REACH + 1):
        both = jnp.concatenate([parts[offset][1], parts[offset][2]], axis=-1)
        both = from_behind(both, "seq", -offset)
        key_back, value_back = both[..., :HD], both[..., HD:]
        key_total = key_total + key_back
        value_total = value_total + value_back
    query_grad = query_total.reshape(tok_rows, -1).astype(jnp.bfloat16)
    key_grad = key_total.reshape(tok_rows, -1).astype(jnp.bfloat16)
    value_grad = value_total.reshape(tok_rows, -1).astype(jnp.bfloat16)
    moe_rows = moe_grad.shape[0]
    capacity = moe_rows * TOP // EXPERTS
    copies = max(1, ep_size // EXPERTS)
    logits = jnp.einsum("td,ed->te", normed, router, preferred_element_type=jnp.float32)
    expert_ids = jnp.arange(EXPERTS, dtype=jnp.int32)
    onehot = (routes[:, :, None] == expert_ids[None, None, :]).astype(jnp.float32)
    chosen = jnp.sum(onehot * logits[:, None, :], axis=2)
    first_gate = 1.0 / (1.0 + jnp.exp(chosen[:, 1] - chosen[:, 0]))
    second_gate = 1.0 - first_gate
    gate_grad = jnp.einsum("td,tkd->tk", moe_grad, expert_out, preferred_element_type=jnp.float32)
    logit_step = first_gate * second_gate * (gate_grad[:, 0] - gate_grad[:, 1])
    logit_grad = (onehot[:, 0, :] - onehot[:, 1, :]) * logit_step[:, None]
    normed_grad = jnp.dot(
        logit_grad, router.astype(jnp.float32), precision=lax.Precision.HIGHEST
    ).astype(jnp.bfloat16)
    local_router = jnp.dot(
        logit_grad.T, normed.astype(jnp.float32), precision=lax.Precision.HIGHEST
    )
    all_tokens = moe_rows * lax.axis_size("seq") * ep_size
    router_grad = sum_everywhere(local_router) / all_tokens
    gates = jnp.stack([first_gate, second_gate], axis=1)
    expert_rows = (gates[:, :, None] * moe_grad.astype(jnp.float32)[:, None, :]).astype(
        jnp.bfloat16
    )
    flat_routes = routes.reshape(-1)
    hot = (flat_routes[:, None] == expert_ids[None, :]).astype(jnp.int32)
    ranks = jnp.sum((jnp.cumsum(hot, axis=0) - 1) * hot, axis=1)
    order = jnp.argsort(flat_routes * capacity + ranks)
    outgoing = expert_rows.reshape(-1, expert_rows.shape[2])[order]
    outgoing = jnp.repeat(outgoing.reshape(EXPERTS, capacity, -1), copies, axis=0)
    router_grad, outgoing = lax.optimization_barrier((router_grad, outgoing))
    routed_grads = lax.all_to_all(outgoing, "ep", split_axis=0, concat_axis=0, tiled=True)
    return (query_grad, key_grad, value_grad, normed_grad, router_grad, routed_grads)


def solution(mesh):
    return jax.shard_map(
        on_device,
        mesh=mesh,
        in_specs=(
            P("seq", "ep"),
            P("seq", "ep"),
            P("seq", "ep"),
            P("seq", "ep"),
            P("seq"),
            P(("seq", "ep"), None),
            P(("seq", "ep"), None, None),
            P(("seq", "ep"), None),
            P(),
            P(("seq", "ep"), None),
        ),
        out_specs=(
            P("seq", "ep"),
            P("seq", "ep"),
            P("seq", "ep"),
            P(("seq", "ep"), None),
            P(),
            P(("seq", "ep"), None, None),
        ),
        check_vma=False,
    )
```

```python
import functools
import math

import jax
import jax.numpy as jnp
from jax import lax
from jax.sharding import PartitionSpec as P

EXPERTS = 8
HD = 128
TOP = 2
REACH = 3


MASKED = -1e30


def from_behind(value, axis, by):
    devices = lax.axis_size(axis)
    pairs = [(i, i + by) for i in range(devices) if 0 <= i + by < devices]
    return lax.ppermute(value, axis, pairs)


def pack_block(key_block, value_block, segments):
    tok_rows = key_block.shape[0]
    width = 2 * key_block.shape[1] * HD
    rows = jnp.concatenate([key_block, value_block], axis=-1).reshape(tok_rows, width)
    segs = segments.astype(jnp.bfloat16).reshape(-1, HD)
    segs = jnp.pad(segs, ((0, 8 - segs.shape[0] % 8), (0, width - HD)))
    return jnp.concatenate([rows, segs], axis=0)


def unpack_block(packed, tok_rows, kv_heads):
    rows = packed[:tok_rows].reshape(tok_rows, kv_heads, 2 * HD)
    segs = packed[tok_rows : tok_rows + tok_rows // HD, :HD].reshape(tok_rows)
    return rows[..., :HD], rows[..., HD:], segs.astype(jnp.int32)


def scatter_sum(flat, axis):
    parts = flat.reshape(lax.axis_size(axis), -1)
    return lax.all_to_all(parts, axis, 0, 0, tiled=True).sum(axis=0)


def gather_back(flat, axis):
    copies = jnp.broadcast_to(flat[None], (lax.axis_size(axis),) + flat.shape)
    return lax.all_to_all(copies, axis, 0, 0, tiled=True).reshape(-1)


def broadcast_sum(flat, axis):
    copies = jnp.broadcast_to(flat[None], (lax.axis_size(axis),) + flat.shape)
    return lax.all_to_all(copies, axis, 0, 0, tiled=True).sum(axis=0)


def sum_everywhere(value):
    flat = broadcast_sum(scatter_sum(value.reshape(-1), "ep"), "seq")
    return gather_back(flat, "ep").reshape(value.shape)


def allowed_pairs(seg_rows, seg_keys, seq_index, offset, tok_rows):
    positions = jnp.arange(tok_rows, dtype=jnp.int32)
    row_pos = seq_index * tok_rows + positions
    key_pos = (seq_index - offset) * tok_rows + positions
    same_doc = seg_rows[:, None] == seg_keys[None, :]
    causal = key_pos[None, :] <= row_pos[:, None]
    return same_doc & causal & (seq_index - offset >= 0)


def masked_scores(query_rows, key_block, allowed, score_scale):
    raw_scores = (
        jnp.einsum("qhgd,thd->hgqt", query_rows, key_block, preferred_element_type=jnp.float32)
        * score_scale
    )
    return jnp.where(allowed, raw_scores, MASKED)


def stats_update(running, query_rows, grad_rows, key_block, value_block, allowed, score_scale):
    row_peak, row_total, weighted = running
    scores = masked_scores(query_rows, key_block, allowed, score_scale)
    prob_grad = jnp.einsum(
        "qhgd,thd->hgqt", grad_rows, value_block, preferred_element_type=jnp.float32
    )
    new_peak = jnp.maximum(row_peak, jnp.max(scores, axis=-1))
    factor = jnp.exp(row_peak - new_peak)
    weights = jnp.where(allowed, jnp.exp(scores - new_peak[..., None]), 0.0)
    return (
        new_peak,
        row_total * factor + jnp.sum(weights, axis=-1),
        weighted * factor + jnp.sum(weights * prob_grad, axis=-1),
    )


def block_grads(
    query_rows, grad_rows, key_block, value_block, allowed, log_total, delta, score_scale
):
    scores = masked_scores(query_rows, key_block, allowed, score_scale)
    soft_probs = jnp.where(allowed, jnp.exp(scores - log_total[..., None]), 0.0)
    probs_low = soft_probs.astype(jnp.bfloat16)
    value_part = jnp.einsum(
        "hgqt,qhgd->thd", probs_low, grad_rows, preferred_element_type=jnp.float32
    )
    prob_grad = jnp.einsum(
        "qhgd,thd->hgqt", grad_rows, value_block, preferred_element_type=jnp.float32
    )
    score_low = (soft_probs * (prob_grad - delta[..., None])).astype(jnp.bfloat16)
    query_part = (
        jnp.einsum("hgqt,thd->qhgd", score_low, key_block, preferred_element_type=jnp.float32)
        * score_scale
    )
    key_part = (
        jnp.einsum("hgqt,qhgd->thd", score_low, query_rows, preferred_element_type=jnp.float32)
        * score_scale
    )
    return (query_part, key_part, value_part)


def on_device(
    queries,
    key_heads,
    value_heads,
    attn_grad,
    segments,
    moe_grad,
    expert_out,
    normed,
    router,
    routes,
):
    tok_rows = queries.shape[0]
    kv_heads = key_heads.shape[1] // HD
    group_size = queries.shape[1] // (kv_heads * HD)
    score_scale = 1.0 / math.sqrt(HD)
    query_rows = queries.reshape(tok_rows, kv_heads, group_size, HD)
    grad_rows = attn_grad.reshape(tok_rows, kv_heads, group_size, HD)
    key_block = key_heads.reshape(tok_rows, kv_heads, HD)
    value_block = value_heads.reshape(tok_rows, kv_heads, HD)
    seq_index = lax.axis_index("seq")
    ep_size = lax.axis_size("ep")
    gathered = [(key_block, value_block, segments)]
    packed = pack_block(key_block, value_block, segments)
    for offset in range(1, REACH + 1):
        gathered.append(unpack_block(from_behind(packed, "seq", offset), tok_rows, kv_heads))
    stat_shape = (kv_heads, group_size, tok_rows)
    running = (
        jnp.full(stat_shape, MASKED, jnp.float32),
        jnp.zeros(stat_shape, jnp.float32),
        jnp.zeros(stat_shape, jnp.float32),
    )
    masks = []
    for offset, (keys_now, values_now, segs_now) in enumerate(gathered):
        allowed = allowed_pairs(segments, segs_now, seq_index, offset, tok_rows)
        masks.append(allowed)
        compute = functools.partial(
            stats_update, running, query_rows, grad_rows, keys_now, values_now, allowed, score_scale
        )
        if offset == 0:
            running = compute()
        else:
            running = compute()
    row_peak, row_total, weighted = running
    log_total = row_peak + jnp.log(row_total)
    delta = weighted / row_total
    def grads_at(offset, rows_q, rows_g, keys_now, values_now):
        return block_grads(
            rows_q, rows_g, keys_now, values_now, masks[offset], log_total, delta, score_scale
        )

    parts = {}
    returned = {}
    for offset in range(REACH, 0, -1):
        keys_now, values_now, _ = gathered[offset]
        parts[offset] = grads_at(offset, query_rows, grad_rows, keys_now, values_now)
        both = jnp.concatenate([parts[offset][1], parts[offset][2]], axis=-1)
        returned[offset] = from_behind(both, "seq", -offset)
    sent = [parts[offset][1:] for offset in range(1, REACH + 1)]
    local_in, _ = lax.optimization_barrier(
        ((query_rows, grad_rows, key_block, value_block), sent)
    )
    parts[0] = grads_at(0, *local_in)
    query_total = parts[0][0]
    for offset in range(1, REACH + 1):
        query_total = query_total + parts[offset][0]
    key_total = parts[0][1]
    value_total = parts[0][2]
    for offset in range(1, REACH + 1):
        both = returned[offset]
        key_back, value_back = both[..., :HD], both[..., HD:]
        key_total = key_total + key_back
        value_total = value_total + value_back
    query_grad = query_total.reshape(tok_rows, -1).astype(jnp.bfloat16)
    key_grad = key_total.reshape(tok_rows, -1).astype(jnp.bfloat16)
    value_grad = value_total.reshape(tok_rows, -1).astype(jnp.bfloat16)
    moe_rows = moe_grad.shape[0]
    capacity = moe_rows * TOP // EXPERTS
    copies = max(1, ep_size // EXPERTS)
    logits = jnp.einsum("td,ed->te", normed, router, preferred_element_type=jnp.float32)
    expert_ids = jnp.arange(EXPERTS, dtype=jnp.int32)
    onehot = (routes[:, :, None] == expert_ids[None, None, :]).astype(jnp.float32)
    chosen = jnp.sum(onehot * logits[:, None, :], axis=2)
    first_gate = 1.0 / (1.0 + jnp.exp(chosen[:, 1] - chosen[:, 0]))
    second_gate = 1.0 - first_gate
    gate_grad = jnp.einsum("td,tkd->tk", moe_grad, expert_out, preferred_element_type=jnp.float32)
    logit_step = first_gate * second_gate * (gate_grad[:, 0] - gate_grad[:, 1])
    logit_grad = (onehot[:, 0, :] - onehot[:, 1, :]) * logit_step[:, None]
    normed_grad = jnp.dot(
        logit_grad, router.astype(jnp.float32), precision=lax.Precision.HIGHEST
    ).astype(jnp.bfloat16)
    local_router = jnp.dot(
        logit_grad.T, normed.astype(jnp.float32), precision=lax.Precision.HIGHEST
    )
    all_tokens = moe_rows * lax.axis_size("seq") * ep_size
    router_grad = sum_everywhere(local_router) / all_tokens
    gates = jnp.stack([first_gate, second_gate], axis=1)
    expert_rows = (gates[:, :, None] * moe_grad.astype(jnp.float32)[:, None, :]).astype(
        jnp.bfloat16
    )
    flat_routes = routes.reshape(-1)
    hot = (flat_routes[:, None] == expert_ids[None, :]).astype(jnp.int32)
    ranks = jnp.sum((jnp.cumsum(hot, axis=0) - 1) * hot, axis=1)
    order = jnp.argsort(flat_routes * capacity + ranks)
    outgoing = expert_rows.reshape(-1, expert_rows.shape[2])[order]
    outgoing = jnp.repeat(outgoing.reshape(EXPERTS, capacity, -1), copies, axis=0)
    router_grad, outgoing = lax.optimization_barrier((router_grad, outgoing))
    routed_grads = lax.all_to_all(outgoing, "ep", split_axis=0, concat_axis=0, tiled=True)
    return (query_grad, key_grad, value_grad, normed_grad, router_grad, routed_grads)


def solution(mesh):
    return jax.shard_map(
        on_device,
        mesh=mesh,
        in_specs=(
            P("seq", "ep"),
            P("seq", "ep"),
            P("seq", "ep"),
            P("seq", "ep"),
            P("seq"),
            P(("seq", "ep"), None),
            P(("seq", "ep"), None, None),
            P(("seq", "ep"), None),
            P(),
            P(("seq", "ep"), None),
        ),
        out_specs=(
            P("seq", "ep"),
            P("seq", "ep"),
            P("seq", "ep"),
            P(("seq", "ep"), None),
            P(),
            P(("seq", "ep"), None, None),
        ),
        check_vma=False,
    )
```

```python
import functools
import math

import jax
import jax.numpy as jnp
from jax import lax
from jax.sharding import PartitionSpec as P

EXPERTS = 8
HD = 128
TOP = 2
REACH = 3


MASKED = -1e30


def from_behind(value, axis, by):
    devices = lax.axis_size(axis)
    pairs = [(i, i + by) for i in range(devices) if 0 <= i + by < devices]
    return lax.ppermute(value, axis, pairs)


def pack_block(key_block, value_block, segments):
    tok_rows = key_block.shape[0]
    width = 2 * key_block.shape[1] * HD
    rows = jnp.concatenate([key_block, value_block], axis=-1).reshape(tok_rows, width)
    segs = segments.astype(jnp.bfloat16).reshape(-1, HD)
    segs = jnp.pad(segs, ((0, 8 - segs.shape[0] % 8), (0, width - HD)))
    return jnp.concatenate([rows, segs], axis=0)


def unpack_block(packed, tok_rows, kv_heads):
    rows = packed[:tok_rows].reshape(tok_rows, kv_heads, 2 * HD)
    segs = packed[tok_rows : tok_rows + tok_rows // HD, :HD].reshape(tok_rows)
    return rows[..., :HD], rows[..., HD:], segs.astype(jnp.int32)


def scatter_sum(flat, axis):
    parts = flat.reshape(lax.axis_size(axis), -1)
    return lax.all_to_all(parts, axis, 0, 0, tiled=True).sum(axis=0)


def gather_back(flat, axis):
    copies = jnp.broadcast_to(flat[None], (lax.axis_size(axis),) + flat.shape)
    return lax.all_to_all(copies, axis, 0, 0, tiled=True).reshape(-1)


def broadcast_sum(flat, axis):
    copies = jnp.broadcast_to(flat[None], (lax.axis_size(axis),) + flat.shape)
    return lax.all_to_all(copies, axis, 0, 0, tiled=True).sum(axis=0)


def sum_everywhere(value):
    flat = broadcast_sum(scatter_sum(value.reshape(-1), "ep"), "seq")
    return gather_back(flat, "ep").reshape(value.shape)


def allowed_pairs(seg_rows, seg_keys, seq_index, offset, tok_rows):
    positions = jnp.arange(tok_rows, dtype=jnp.int32)
    row_pos = seq_index * tok_rows + positions
    key_pos = (seq_index - offset) * tok_rows + positions
    same_doc = seg_rows[:, None] == seg_keys[None, :]
    causal = key_pos[None, :] <= row_pos[:, None]
    return same_doc & causal & (seq_index - offset >= 0)


def masked_scores(query_rows, key_block, allowed, score_scale):
    raw_scores = (
        jnp.einsum("qhgd,thd->hgqt", query_rows, key_block, preferred_element_type=jnp.float32)
        * score_scale
    )
    return jnp.where(allowed, raw_scores, MASKED)


def stats_update(running, query_rows, grad_rows, key_block, value_block, allowed, score_scale):
    row_peak, row_total, weighted = running
    scores = masked_scores(query_rows, key_block, allowed, score_scale)
    prob_grad = jnp.einsum(
        "qhgd,thd->hgqt", grad_rows, value_block, preferred_element_type=jnp.float32
    )
    new_peak = jnp.maximum(row_peak, jnp.max(scores, axis=-1))
    factor = jnp.exp(row_peak - new_peak)
    weights = jnp.where(allowed, jnp.exp(scores - new_peak[..., None]), 0.0)
    return (
        new_peak,
        row_total * factor + jnp.sum(weights, axis=-1),
        weighted * factor + jnp.sum(weights * prob_grad, axis=-1),
    )


def block_grads(
    query_rows, grad_rows, key_block, value_block, allowed, log_total, delta, score_scale
):
    scores = masked_scores(query_rows, key_block, allowed, score_scale)
    soft_probs = jnp.where(allowed, jnp.exp(scores - log_total[..., None]), 0.0)
    probs_low = soft_probs.astype(jnp.bfloat16)
    value_part = jnp.einsum(
        "hgqt,qhgd->thd", probs_low, grad_rows, preferred_element_type=jnp.float32
    )
    prob_grad = jnp.einsum(
        "qhgd,thd->hgqt", grad_rows, value_block, preferred_element_type=jnp.float32
    )
    score_low = (soft_probs * (prob_grad - delta[..., None])).astype(jnp.bfloat16)
    query_part = (
        jnp.einsum("hgqt,thd->qhgd", score_low, key_block, preferred_element_type=jnp.float32)
        * score_scale
    )
    key_part = (
        jnp.einsum("hgqt,qhgd->thd", score_low, query_rows, preferred_element_type=jnp.float32)
        * score_scale
    )
    return (query_part, key_part, value_part)


def on_device(
    queries,
    key_heads,
    value_heads,
    attn_grad,
    segments,
    moe_grad,
    expert_out,
    normed,
    router,
    routes,
):
    tok_rows = queries.shape[0]
    kv_heads = key_heads.shape[1] // HD
    group_size = queries.shape[1] // (kv_heads * HD)
    score_scale = 1.0 / math.sqrt(HD)
    query_rows = queries.reshape(tok_rows, kv_heads, group_size, HD)
    grad_rows = attn_grad.reshape(tok_rows, kv_heads, group_size, HD)
    key_block = key_heads.reshape(tok_rows, kv_heads, HD)
    value_block = value_heads.reshape(tok_rows, kv_heads, HD)
    seq_index = lax.axis_index("seq")
    ep_size = lax.axis_size("ep")
    gathered = [(key_block, value_block, segments)]
    packed = pack_block(key_block, value_block, segments)
    for offset in range(1, REACH + 1):
        gathered.append(unpack_block(from_behind(packed, "seq", offset), tok_rows, kv_heads))
    stat_shape = (kv_heads, group_size, tok_rows)
    running = (
        jnp.full(stat_shape, MASKED, jnp.float32),
        jnp.zeros(stat_shape, jnp.float32),
        jnp.zeros(stat_shape, jnp.float32),
    )
    masks = []
    for offset, (keys_now, values_now, segs_now) in enumerate(gathered):
        allowed = allowed_pairs(segments, segs_now, seq_index, offset, tok_rows)
        masks.append(allowed)
        compute = functools.partial(
            stats_update, running, query_rows, grad_rows, keys_now, values_now, allowed, score_scale
        )
        if offset == 0:
            running = compute()
        else:
            running = compute()
    row_peak, row_total, weighted = running
    log_total = row_peak + jnp.log(row_total)
    delta = weighted / row_total
    def grads_at(offset, rows_q, rows_g, keys_now, values_now):
        return block_grads(
            rows_q, rows_g, keys_now, values_now, masks[offset], log_total, delta, score_scale
        )

    parts = {}
    returned = {}
    for offset in range(REACH, 0, -1):
        keys_now, values_now, _ = gathered[offset]
        parts[offset] = grads_at(offset, query_rows, grad_rows, keys_now, values_now)
        both = jnp.concatenate([parts[offset][1], parts[offset][2]], axis=-1)
        returned[offset] = from_behind(both, "seq", -offset)
    sent = [parts[offset][1:] for offset in range(1, REACH + 1)]
    local_in, _ = lax.optimization_barrier(
        ((query_rows, grad_rows, key_block, value_block), sent)
    )
    parts[0] = grads_at(0, *local_in)
    query_total = parts[0][0]
    for offset in range(1, REACH + 1):
        query_total = query_total + parts[offset][0]
    key_total = parts[0][1]
    value_total = parts[0][2]
    for offset in range(1, REACH + 1):
        both = returned[offset]
        key_back, value_back = both[..., :HD], both[..., HD:]
        key_total = key_total + key_back
        value_total = value_total + value_back
    query_grad = query_total.reshape(tok_rows, -1).astype(jnp.bfloat16)
    key_grad = key_total.reshape(tok_rows, -1).astype(jnp.bfloat16)
    value_grad = value_total.reshape(tok_rows, -1).astype(jnp.bfloat16)
    moe_rows = moe_grad.shape[0]
    capacity = moe_rows * TOP // EXPERTS
    copies = max(1, ep_size // EXPERTS)
    logits = jnp.einsum("td,ed->te", normed, router, preferred_element_type=jnp.float32)
    expert_ids = jnp.arange(EXPERTS, dtype=jnp.int32)
    onehot = (routes[:, :, None] == expert_ids[None, None, :]).astype(jnp.float32)
    chosen = jnp.sum(onehot * logits[:, None, :], axis=2)
    first_gate = 1.0 / (1.0 + jnp.exp(chosen[:, 1] - chosen[:, 0]))
    second_gate = 1.0 - first_gate
    gate_grad = jnp.einsum("td,tkd->tk", moe_grad, expert_out, preferred_element_type=jnp.float32)
    logit_step = first_gate * second_gate * (gate_grad[:, 0] - gate_grad[:, 1])
    logit_grad = (onehot[:, 0, :] - onehot[:, 1, :]) * logit_step[:, None]
    normed_grad = jnp.dot(
        logit_grad, router.astype(jnp.float32), precision=lax.Precision.HIGHEST
    ).astype(jnp.bfloat16)
    local_router = jnp.dot(
        logit_grad.T, normed.astype(jnp.float32), precision=lax.Precision.HIGHEST
    )
    all_tokens = moe_rows * lax.axis_size("seq") * ep_size
    gates = jnp.stack([first_gate, second_gate], axis=1)
    expert_rows = (gates[:, :, None] * moe_grad.astype(jnp.float32)[:, None, :]).astype(
        jnp.bfloat16
    )
    flat_routes = routes.reshape(-1)
    hot = (flat_routes[:, None] == expert_ids[None, :]).astype(jnp.int32)
    ranks = jnp.sum((jnp.cumsum(hot, axis=0) - 1) * hot, axis=1)
    order = jnp.argsort(flat_routes * capacity + ranks)
    outgoing = expert_rows.reshape(-1, expert_rows.shape[2])[order]
    outgoing = jnp.repeat(outgoing.reshape(EXPERTS, capacity, -1), copies, axis=0)
    slots = outgoing.shape[0]
    router_parts = local_router.reshape(slots, -1)
    merged = jnp.concatenate(
        [outgoing.reshape(slots, -1).astype(jnp.float32), router_parts], axis=1
    )
    merged = lax.all_to_all(merged, "ep", split_axis=0, concat_axis=0, tiled=True)
    split_at = merged.shape[1] - router_parts.shape[1]
    routed_grads = merged[:, :split_at].reshape(outgoing.shape).astype(jnp.bfloat16)
    router_flat = broadcast_sum(merged[:, split_at:].sum(axis=0), "seq")
    router_grad = gather_back(router_flat, "ep").reshape(local_router.shape) / all_tokens
    return (query_grad, key_grad, value_grad, normed_grad, router_grad, routed_grads)


def solution(mesh):
    return jax.shard_map(
        on_device,
        mesh=mesh,
        in_specs=(
            P("seq", "ep"),
            P("seq", "ep"),
            P("seq", "ep"),
            P("seq", "ep"),
            P("seq"),
            P(("seq", "ep"), None),
            P(("seq", "ep"), None, None),
            P(("seq", "ep"), None),
            P(),
            P(("seq", "ep"), None),
        ),
        out_specs=(
            P("seq", "ep"),
            P("seq", "ep"),
            P("seq", "ep"),
            P(("seq", "ep"), None),
            P(),
            P(("seq", "ep"), None, None),
        ),
        check_vma=False,
    )
```

```python
import functools
import math

import jax
import jax.numpy as jnp
from jax import lax
from jax.sharding import PartitionSpec as P

EXPERTS = 8
HD = 128
TOP = 2
REACH = 3


MASKED = -1e30


def from_behind(value, axis, by):
    devices = lax.axis_size(axis)
    pairs = [(i, i + by) for i in range(devices) if 0 <= i + by < devices]
    return lax.ppermute(value, axis, pairs)


def pack_block(key_block, value_block, segments):
    tok_rows = key_block.shape[0]
    width = 2 * key_block.shape[1] * HD
    rows = jnp.concatenate([key_block, value_block], axis=-1).reshape(tok_rows, width)
    segs = segments.astype(jnp.bfloat16).reshape(-1, HD)
    segs = jnp.pad(segs, ((0, 8 - segs.shape[0] % 8), (0, width - HD)))
    return jnp.concatenate([rows, segs], axis=0)


def unpack_block(packed, tok_rows, kv_heads):
    rows = packed[:tok_rows].reshape(tok_rows, kv_heads, 2 * HD)
    segs = packed[tok_rows : tok_rows + tok_rows // HD, :HD].reshape(tok_rows)
    return rows[..., :HD], rows[..., HD:], segs.astype(jnp.int32)


def scatter_sum(flat, axis):
    parts = flat.reshape(lax.axis_size(axis), -1)
    return lax.all_to_all(parts, axis, 0, 0, tiled=True).sum(axis=0)


def gather_back(flat, axis):
    copies = jnp.broadcast_to(flat[None], (lax.axis_size(axis),) + flat.shape)
    return lax.all_to_all(copies, axis, 0, 0, tiled=True).reshape(-1)


def broadcast_sum(flat, axis):
    copies = jnp.broadcast_to(flat[None], (lax.axis_size(axis),) + flat.shape)
    return lax.all_to_all(copies, axis, 0, 0, tiled=True).sum(axis=0)


def sum_everywhere(value):
    flat = broadcast_sum(scatter_sum(value.reshape(-1), "ep"), "seq")
    return gather_back(flat, "ep").reshape(value.shape)


def allowed_pairs(seg_rows, seg_keys, seq_index, offset, tok_rows):
    positions = jnp.arange(tok_rows, dtype=jnp.int32)
    row_pos = seq_index * tok_rows + positions
    key_pos = (seq_index - offset) * tok_rows + positions
    same_doc = seg_rows[:, None] == seg_keys[None, :]
    causal = key_pos[None, :] <= row_pos[:, None]
    return same_doc & causal & (seq_index - offset >= 0)


def masked_scores(query_rows, key_block, allowed, score_scale):
    raw_scores = (
        jnp.einsum("qhgd,thd->hgqt", query_rows, key_block, preferred_element_type=jnp.float32)
        * score_scale
    )
    return jnp.where(allowed, raw_scores, MASKED)


def stats_update(running, query_rows, grad_rows, key_block, value_block, allowed, score_scale):
    row_peak, row_total, weighted = running
    scores = masked_scores(query_rows, key_block, allowed, score_scale)
    prob_grad = jnp.einsum(
        "qhgd,thd->hgqt", grad_rows, value_block, preferred_element_type=jnp.float32
    )
    new_peak = jnp.maximum(row_peak, jnp.max(scores, axis=-1))
    factor = jnp.exp(row_peak - new_peak)
    weights = jnp.where(allowed, jnp.exp(scores - new_peak[..., None]), 0.0)
    return (
        new_peak,
        row_total * factor + jnp.sum(weights, axis=-1),
        weighted * factor + jnp.sum(weights * prob_grad, axis=-1),
    )


def block_grads(
    query_rows, grad_rows, key_block, value_block, allowed, log_total, delta, score_scale
):
    scores = masked_scores(query_rows, key_block, allowed, score_scale)
    soft_probs = jnp.where(allowed, jnp.exp(scores - log_total[..., None]), 0.0)
    probs_low = soft_probs.astype(jnp.bfloat16)
    value_part = jnp.einsum(
        "hgqt,qhgd->thd", probs_low, grad_rows, preferred_element_type=jnp.float32
    )
    prob_grad = jnp.einsum(
        "qhgd,thd->hgqt", grad_rows, value_block, preferred_element_type=jnp.float32
    )
    score_low = (soft_probs * (prob_grad - delta[..., None])).astype(jnp.bfloat16)
    query_part = (
        jnp.einsum("hgqt,thd->qhgd", score_low, key_block, preferred_element_type=jnp.float32)
        * score_scale
    )
    key_part = (
        jnp.einsum("hgqt,qhgd->thd", score_low, query_rows, preferred_element_type=jnp.float32)
        * score_scale
    )
    return (query_part, key_part, value_part)


def on_device(
    queries,
    key_heads,
    value_heads,
    attn_grad,
    segments,
    moe_grad,
    expert_out,
    normed,
    router,
    routes,
):
    tok_rows = queries.shape[0]
    kv_heads = key_heads.shape[1] // HD
    group_size = queries.shape[1] // (kv_heads * HD)
    score_scale = 1.0 / math.sqrt(HD)
    query_rows = queries.reshape(tok_rows, kv_heads, group_size, HD)
    grad_rows = attn_grad.reshape(tok_rows, kv_heads, group_size, HD)
    key_block = key_heads.reshape(tok_rows, kv_heads, HD)
    value_block = value_heads.reshape(tok_rows, kv_heads, HD)
    seq_index = lax.axis_index("seq")
    ep_size = lax.axis_size("ep")
    gathered = [(key_block, value_block, segments)]
    moe_rows = moe_grad.shape[0]
    capacity = moe_rows * TOP // EXPERTS
    copies = max(1, ep_size // EXPERTS)
    logits = jnp.einsum("td,ed->te", normed, router, preferred_element_type=jnp.float32)
    expert_ids = jnp.arange(EXPERTS, dtype=jnp.int32)
    onehot = (routes[:, :, None] == expert_ids[None, None, :]).astype(jnp.float32)
    chosen = jnp.sum(onehot * logits[:, None, :], axis=2)
    first_gate = 1.0 / (1.0 + jnp.exp(chosen[:, 1] - chosen[:, 0]))
    second_gate = 1.0 - first_gate
    gate_grad = jnp.einsum("td,tkd->tk", moe_grad, expert_out, preferred_element_type=jnp.float32)
    logit_step = first_gate * second_gate * (gate_grad[:, 0] - gate_grad[:, 1])
    logit_grad = (onehot[:, 0, :] - onehot[:, 1, :]) * logit_step[:, None]
    normed_grad = jnp.dot(
        logit_grad, router.astype(jnp.float32), precision=lax.Precision.HIGHEST
    ).astype(jnp.bfloat16)
    local_router = jnp.dot(
        logit_grad.T, normed.astype(jnp.float32), precision=lax.Precision.HIGHEST
    )
    packed = pack_block(key_block, value_block, segments)
    local_router, packed = lax.optimization_barrier((local_router, packed))
    for offset in range(1, REACH + 1):
        gathered.append(unpack_block(from_behind(packed, "seq", offset), tok_rows, kv_heads))
    stat_shape = (kv_heads, group_size, tok_rows)
    running = (
        jnp.full(stat_shape, MASKED, jnp.float32),
        jnp.zeros(stat_shape, jnp.float32),
        jnp.zeros(stat_shape, jnp.float32),
    )
    masks = []
    for offset, (keys_now, values_now, segs_now) in enumerate(gathered):
        allowed = allowed_pairs(segments, segs_now, seq_index, offset, tok_rows)
        masks.append(allowed)
        compute = functools.partial(
            stats_update, running, query_rows, grad_rows, keys_now, values_now, allowed, score_scale
        )
        if offset == 0:
            running = compute()
        else:
            running = compute()
    row_peak, row_total, weighted = running
    log_total = row_peak + jnp.log(row_total)
    delta = weighted / row_total
    def grads_at(offset, rows_q, rows_g, keys_now, values_now):
        return block_grads(
            rows_q, rows_g, keys_now, values_now, masks[offset], log_total, delta, score_scale
        )

    parts = {}
    returned = {}
    for offset in range(REACH, 0, -1):
        keys_now, values_now, _ = gathered[offset]
        parts[offset] = grads_at(offset, query_rows, grad_rows, keys_now, values_now)
        both = jnp.concatenate([parts[offset][1], parts[offset][2]], axis=-1)
        returned[offset] = from_behind(both, "seq", -offset)
    sent = [parts[offset][1:] for offset in range(1, REACH + 1)]
    local_in, _ = lax.optimization_barrier(
        ((query_rows, grad_rows, key_block, value_block), sent)
    )
    parts[0] = grads_at(0, *local_in)
    query_total = parts[0][0]
    for offset in range(1, REACH + 1):
        query_total = query_total + parts[offset][0]
    key_total = parts[0][1]
    value_total = parts[0][2]
    for offset in range(1, REACH + 1):
        both = returned[offset]
        key_back, value_back = both[..., :HD], both[..., HD:]
        key_total = key_total + key_back
        value_total = value_total + value_back
    query_grad = query_total.reshape(tok_rows, -1).astype(jnp.bfloat16)
    key_grad = key_total.reshape(tok_rows, -1).astype(jnp.bfloat16)
    value_grad = value_total.reshape(tok_rows, -1).astype(jnp.bfloat16)
    all_tokens = moe_rows * lax.axis_size("seq") * ep_size
    router_grad = sum_everywhere(local_router) / all_tokens
    gates = jnp.stack([first_gate, second_gate], axis=1)
    expert_rows = (gates[:, :, None] * moe_grad.astype(jnp.float32)[:, None, :]).astype(
        jnp.bfloat16
    )
    flat_routes = routes.reshape(-1)
    hot = (flat_routes[:, None] == expert_ids[None, :]).astype(jnp.int32)
    ranks = jnp.sum((jnp.cumsum(hot, axis=0) - 1) * hot, axis=1)
    order = jnp.argsort(flat_routes * capacity + ranks)
    outgoing = expert_rows.reshape(-1, expert_rows.shape[2])[order]
    outgoing = jnp.repeat(outgoing.reshape(EXPERTS, capacity, -1), copies, axis=0)
    router_grad, outgoing = lax.optimization_barrier((router_grad, outgoing))
    routed_grads = lax.all_to_all(outgoing, "ep", split_axis=0, concat_axis=0, tiled=True)
    return (query_grad, key_grad, value_grad, normed_grad, router_grad, routed_grads)


def solution(mesh):
    return jax.shard_map(
        on_device,
        mesh=mesh,
        in_specs=(
            P("seq", "ep"),
            P("seq", "ep"),
            P("seq", "ep"),
            P("seq", "ep"),
            P("seq"),
            P(("seq", "ep"), None),
            P(("seq", "ep"), None, None),
            P(("seq", "ep"), None),
            P(),
            P(("seq", "ep"), None),
        ),
        out_specs=(
            P("seq", "ep"),
            P("seq", "ep"),
            P("seq", "ep"),
            P(("seq", "ep"), None),
            P(),
            P(("seq", "ep"), None, None),
        ),
        check_vma=False,
    )
```

```python
import functools
import math

import jax
import jax.numpy as jnp
from jax import lax
from jax.sharding import PartitionSpec as P

EXPERTS = 8
HD = 128
TOP = 2
REACH = 3


MASKED = -1e30


def from_behind(value, axis, by):
    devices = lax.axis_size(axis)
    pairs = [(i, i + by) for i in range(devices) if 0 <= i + by < devices]
    return lax.ppermute(value, axis, pairs)


def pack_block(key_block, value_block, segments):
    tok_rows = key_block.shape[0]
    width = 2 * key_block.shape[1] * HD
    rows = jnp.concatenate([key_block, value_block], axis=-1).reshape(tok_rows, width)
    segs = segments.astype(jnp.bfloat16).reshape(-1, HD)
    segs = jnp.pad(segs, ((0, 8 - segs.shape[0] % 8), (0, width - HD)))
    return jnp.concatenate([rows, segs], axis=0)


def unpack_block(packed, tok_rows, kv_heads):
    rows = packed[:tok_rows].reshape(tok_rows, kv_heads, 2 * HD)
    segs = packed[tok_rows : tok_rows + tok_rows // HD, :HD].reshape(tok_rows)
    return rows[..., :HD], rows[..., HD:], segs.astype(jnp.int32)


def scatter_sum(flat, axis):
    parts = flat.reshape(lax.axis_size(axis), -1)
    return lax.all_to_all(parts, axis, 0, 0, tiled=True).sum(axis=0)


def gather_back(flat, axis):
    copies = jnp.broadcast_to(flat[None], (lax.axis_size(axis),) + flat.shape)
    return lax.all_to_all(copies, axis, 0, 0, tiled=True).reshape(-1)


def broadcast_sum(flat, axis):
    copies = jnp.broadcast_to(flat[None], (lax.axis_size(axis),) + flat.shape)
    return lax.all_to_all(copies, axis, 0, 0, tiled=True).sum(axis=0)


def sum_everywhere(value):
    flat = broadcast_sum(scatter_sum(value.reshape(-1), "ep"), "seq")
    return gather_back(flat, "ep").reshape(value.shape)


def allowed_pairs(seg_rows, seg_keys, seq_index, offset, tok_rows):
    positions = jnp.arange(tok_rows, dtype=jnp.int32)
    row_pos = seq_index * tok_rows + positions
    key_pos = (seq_index - offset) * tok_rows + positions
    same_doc = seg_rows[:, None] == seg_keys[None, :]
    causal = key_pos[None, :] <= row_pos[:, None]
    return same_doc & causal & (seq_index - offset >= 0)


def masked_scores(query_rows, key_block, allowed, score_scale):
    raw_scores = (
        jnp.einsum("qhgd,thd->hgqt", query_rows, key_block, preferred_element_type=jnp.float32)
        * score_scale
    )
    return jnp.where(allowed, raw_scores, MASKED)


def stats_update(running, query_rows, grad_rows, key_block, value_block, allowed, score_scale):
    row_peak, row_total, weighted = running
    scores = masked_scores(query_rows, key_block, allowed, score_scale)
    prob_grad = jnp.einsum(
        "qhgd,thd->hgqt", grad_rows, value_block, preferred_element_type=jnp.float32
    )
    new_peak = jnp.maximum(row_peak, jnp.max(scores, axis=-1))
    factor = jnp.exp(row_peak - new_peak)
    weights = jnp.where(allowed, jnp.exp(scores - new_peak[..., None]), 0.0)
    return (
        new_peak,
        row_total * factor + jnp.sum(weights, axis=-1),
        weighted * factor + jnp.sum(weights * prob_grad, axis=-1),
    )


def block_grads(
    query_rows, grad_rows, key_block, value_block, allowed, log_total, delta, score_scale
):
    scores = masked_scores(query_rows, key_block, allowed, score_scale)
    soft_probs = jnp.where(allowed, jnp.exp(scores - log_total[..., None]), 0.0)
    probs_low = soft_probs.astype(jnp.bfloat16)
    value_part = jnp.einsum(
        "hgqt,qhgd->thd", probs_low, grad_rows, preferred_element_type=jnp.float32
    )
    prob_grad = jnp.einsum(
        "qhgd,thd->hgqt", grad_rows, value_block, preferred_element_type=jnp.float32
    )
    score_low = (soft_probs * (prob_grad - delta[..., None])).astype(jnp.bfloat16)
    query_part = (
        jnp.einsum("hgqt,thd->qhgd", score_low, key_block, preferred_element_type=jnp.float32)
        * score_scale
    )
    key_part = (
        jnp.einsum("hgqt,qhgd->thd", score_low, query_rows, preferred_element_type=jnp.float32)
        * score_scale
    )
    return (query_part, key_part, value_part)


def on_device(
    queries,
    key_heads,
    value_heads,
    attn_grad,
    segments,
    moe_grad,
    expert_out,
    normed,
    router,
    routes,
):
    tok_rows = queries.shape[0]
    kv_heads = key_heads.shape[1] // HD
    group_size = queries.shape[1] // (kv_heads * HD)
    score_scale = 1.0 / math.sqrt(HD)
    query_rows = queries.reshape(tok_rows, kv_heads, group_size, HD)
    grad_rows = attn_grad.reshape(tok_rows, kv_heads, group_size, HD)
    key_block = key_heads.reshape(tok_rows, kv_heads, HD)
    value_block = value_heads.reshape(tok_rows, kv_heads, HD)
    seq_index = lax.axis_index("seq")
    ep_size = lax.axis_size("ep")
    gathered = [(key_block, value_block, segments)]
    moe_rows = moe_grad.shape[0]
    capacity = moe_rows * TOP // EXPERTS
    copies = max(1, ep_size // EXPERTS)
    logits = jnp.einsum("td,ed->te", normed, router, preferred_element_type=jnp.float32)
    expert_ids = jnp.arange(EXPERTS, dtype=jnp.int32)
    onehot = (routes[:, :, None] == expert_ids[None, None, :]).astype(jnp.float32)
    chosen = jnp.sum(onehot * logits[:, None, :], axis=2)
    first_gate = 1.0 / (1.0 + jnp.exp(chosen[:, 1] - chosen[:, 0]))
    second_gate = 1.0 - first_gate
    gate_grad = jnp.einsum("td,tkd->tk", moe_grad, expert_out, preferred_element_type=jnp.float32)
    logit_step = first_gate * second_gate * (gate_grad[:, 0] - gate_grad[:, 1])
    logit_grad = (onehot[:, 0, :] - onehot[:, 1, :]) * logit_step[:, None]
    normed_grad = jnp.dot(
        logit_grad, router.astype(jnp.float32), precision=lax.Precision.HIGHEST
    ).astype(jnp.bfloat16)
    local_router = jnp.dot(
        logit_grad.T, normed.astype(jnp.float32), precision=lax.Precision.HIGHEST
    )
    packed = pack_block(key_block, value_block, segments)
    local_router, packed = lax.optimization_barrier((local_router, packed))
    for offset in range(1, REACH + 1):
        gathered.append(unpack_block(from_behind(packed, "seq", offset), tok_rows, kv_heads))
    stat_shape = (kv_heads, group_size, tok_rows)
    running = (
        jnp.full(stat_shape, MASKED, jnp.float32),
        jnp.zeros(stat_shape, jnp.float32),
        jnp.zeros(stat_shape, jnp.float32),
    )
    masks = []
    for offset, (keys_now, values_now, segs_now) in enumerate(gathered):
        allowed = allowed_pairs(segments, segs_now, seq_index, offset, tok_rows)
        masks.append(allowed)
        compute = functools.partial(
            stats_update, running, query_rows, grad_rows, keys_now, values_now, allowed, score_scale
        )
        if offset == 0:
            running = compute()
        else:
            running = compute()
    row_peak, row_total, weighted = running
    log_total = row_peak + jnp.log(row_total)
    delta = weighted / row_total
    def grads_at(offset, rows_q, rows_g, keys_now, values_now):
        return block_grads(
            rows_q, rows_g, keys_now, values_now, masks[offset], log_total, delta, score_scale
        )

    parts = {}
    returned = {}
    for offset in range(REACH, 0, -1):
        keys_now, values_now, _ = gathered[offset]
        parts[offset] = grads_at(offset, query_rows, grad_rows, keys_now, values_now)
        both = jnp.concatenate([parts[offset][1], parts[offset][2]], axis=-1)
        returned[offset] = from_behind(both, "seq", -offset)
    sent = [parts[offset][1:] for offset in range(1, REACH + 1)]
    local_in, _ = lax.optimization_barrier(
        ((query_rows, grad_rows, key_block, value_block), sent)
    )
    parts[0] = grads_at(0, *local_in)
    query_total = parts[0][0]
    for offset in range(1, REACH + 1):
        query_total = query_total + parts[offset][0]
    key_total = parts[0][1]
    value_total = parts[0][2]
    for offset in range(1, REACH + 1):
        both = returned[offset]
        key_back, value_back = both[..., :HD], both[..., HD:]
        key_total = key_total + key_back
        value_total = value_total + value_back
    query_grad = query_total.reshape(tok_rows, -1).astype(jnp.bfloat16)
    key_grad = key_total.reshape(tok_rows, -1).astype(jnp.bfloat16)
    value_grad = value_total.reshape(tok_rows, -1).astype(jnp.bfloat16)
    all_tokens = moe_rows * lax.axis_size("seq") * ep_size
    router_flat = broadcast_sum(scatter_sum(local_router.reshape(-1), "ep"), "seq")
    gates = jnp.stack([first_gate, second_gate], axis=1)
    expert_rows = (gates[:, :, None] * moe_grad.astype(jnp.float32)[:, None, :]).astype(
        jnp.bfloat16
    )
    flat_routes = routes.reshape(-1)
    hot = (flat_routes[:, None] == expert_ids[None, :]).astype(jnp.int32)
    ranks = jnp.sum((jnp.cumsum(hot, axis=0) - 1) * hot, axis=1)
    order = jnp.argsort(flat_routes * capacity + ranks)
    outgoing = expert_rows.reshape(-1, expert_rows.shape[2])[order]
    outgoing = jnp.repeat(outgoing.reshape(EXPERTS, capacity, -1), copies, axis=0)
    slots = outgoing.shape[0]
    merged = jnp.concatenate(
        [
            outgoing.reshape(slots, -1).astype(jnp.float32),
            jnp.broadcast_to(router_flat[None], (slots,) + router_flat.shape),
        ],
        axis=1,
    )
    merged = lax.all_to_all(merged, "ep", split_axis=0, concat_axis=0, tiled=True)
    split_at = merged.shape[1] - router_flat.shape[0]
    routed_grads = merged[:, :split_at].reshape(outgoing.shape).astype(jnp.bfloat16)
    router_grad = merged[:, split_at:].reshape(local_router.shape) / all_tokens
    return (query_grad, key_grad, value_grad, normed_grad, router_grad, routed_grads)


def solution(mesh):
    return jax.shard_map(
        on_device,
        mesh=mesh,
        in_specs=(
            P("seq", "ep"),
            P("seq", "ep"),
            P("seq", "ep"),
            P("seq", "ep"),
            P("seq"),
            P(("seq", "ep"), None),
            P(("seq", "ep"), None, None),
            P(("seq", "ep"), None),
            P(),
            P(("seq", "ep"), None),
        ),
        out_specs=(
            P("seq", "ep"),
            P("seq", "ep"),
            P("seq", "ep"),
            P(("seq", "ep"), None),
            P(),
            P(("seq", "ep"), None, None),
        ),
        check_vma=False,
    )
```
